256 devices in a mesh: seg: 8 (over x_hi, y), dir: 32 (over z, x_lo, core).
Axes of the slice: x: 4 (x_hi: 2, x_lo: 2; x = x_hi * 2 + x_lo), y: 4, z: 8, core: 2. Of those that a mesh axis runs over, the one named last changes fastest.
Arguments:
- panel: bfloat16 [64, 45056], P('dir'), may hold values from -6 to 6
- seeds: bfloat16 [8, 64, 45056], P('seg', 'dir'), may hold values from -6 to 6
- inverses: bfloat16 [8, 352, 128, 128], P('seg', 'dir'), may hold values from -1 to 1
- coupling: bfloat16 [8, 3, 128, 128], P('seg'), may hold values from -0.5 to 0.5
- weights: float32 [352, 3], replicated, may hold values from -0.3 to 0.3
- pattern: int32 [352, 3], replicated, may hold values from 0 to 351
- counts: int32 [8], replicated, may hold values from 1 to 2, as said below
Outputs:
- tangent: bfloat16 [8, 64, 45056], P('seg', 'dir')
- adjoint: bfloat16 [8, 64, 45056], P('seg', 'dir')
- projected: float32 [64, 64], P('dir')
The draws below stay inside these ranges and needn't reach their ends.
Inputs may be any that keep to these rules, and one draw needn't show every extreme that they name: `counts`: some segment takes 2 time steps.
All inputs are finite; a program needn't handle non-finite values.
Results may differ from the reference program's by a relative error of at most 0.019.
Values may be sent and summed in bfloat16 or wider, within the bound.
No kernel may reach another device: no remote copies, remote signals or barrier semaphores. Data moves between devices by JAX's collectives and lax.ppermute only.
A program may use at most 64 MiB of HBM per device.

```python
import math
import jax
import jax.numpy as jnp

NB = 352
BLOCK = 128
COUPLE = 3
STEPS_MAX = 2
DIRS = 64
SEGS = 8
NS = 45056


def draw_inverses(key, part):
    diag_key, off_key = jax.random.split(jax.random.fold_in(key, 17))
    diagonal = jax.random.uniform(diag_key, (SEGS, NB, BLOCK), jnp.float32, 0.7, 0.88)
    spread = 0.35
    off_part = jax.random.uniform(off_key, (SEGS, NB, BLOCK, BLOCK), jnp.float32, -1.0, 1.0) * (spread * BLOCK ** (-0.5))
    identity = jnp.eye(BLOCK, dtype=jnp.float32)
    return (off_part + diagonal[..., None] * identity).astype(jnp.bfloat16)


def draw_counts(key, part):
    first_key, second_key = jax.random.split(jax.random.fold_in(key, 23))
    steps_drawn = jax.random.randint(first_key, (SEGS,), 1, STEPS_MAX + 1)
    longest = jax.random.randint(second_key, (), 0, SEGS)
    return steps_drawn.at[longest].set(STEPS_MAX).astype(jnp.int32)


def set_ends(drawn, stream_key, smallest, top_value):
    spot = [jax.random.randint(jax.random.fold_in(stream_key, axis), (), 0, length) for axis, length in enumerate(drawn.shape)]
    main_axis = drawn.shape.index(max(drawn.shape))
    neighbour = spot[:main_axis] + [(spot[main_axis] + 1) % drawn.shape[main_axis]] + spot[main_axis + 1:]
    return drawn.at[tuple(spot)].set(smallest).at[tuple(neighbour)].set(top_value)


def shard_levels(stream_key, extent, cuts, least, top_value):
    factor_of = 1.0
    for dim, shards_of in cuts:
        steps = jax.random.uniform(jax.random.fold_in(jax.random.fold_in(stream_key, 6), dim), (shards_of,), jnp.float32, least / len(cuts), top_value / len(cuts))
        factor_of = factor_of * jnp.repeat(jnp.exp(steps), extent[dim] // shards_of).reshape((-1,) + (1,) * (len(extent) - 1 - dim))
    return factor_of


def noise(stream_key, dims, deviation, reach, pieces=(), kind=jnp.bfloat16):
    factor_of = shard_levels(stream_key, dims, pieces, -0.22, 0.18) if pieces else 1.0
    result = jax.random.normal(stream_key, dims, jnp.float32) * deviation * factor_of
    return jnp.minimum(jnp.maximum(result, -reach), reach).astype(kind)


def setup_inputs(seed: int = 0) -> dict:
    key_list = jax.random.split(jax.random.key(seed), 8)
    panel = noise(key_list[0], (DIRS, NS), 1.0, 6.0, ((0, 32),))
    seeds = noise(key_list[1], (SEGS, DIRS, NS), 1.0, 6.0, ((0, 8), (1, 32)))
    inverses = draw_inverses(jax.random.fold_in(key_list[7], 71), 0)
    coupling = noise(key_list[3], (SEGS, COUPLE, BLOCK, BLOCK), BLOCK ** -0.5, 0.5, ((0, 8),))
    weights = jnp.clip(jax.random.uniform(key_list[4], (NB, COUPLE), jnp.float32, -0.3, 0.3), -0.3, 0.3)
    pattern = set_ends(jax.random.randint(key_list[5], (NB, COUPLE), 0, NB), jax.random.fold_in(key_list[5], 1), 0, NB - 1).astype(jnp.int32)
    counts = draw_counts(jax.random.fold_in(key_list[7], 71), 0)
    return {"panel": panel, "seeds": seeds, "inverses": inverses, "coupling": coupling, "weights": weights, "pattern": pattern, "counts": counts}


def step_forward(current, inverse_table, coupling, weights, pattern):
    picked = current[:, pattern, :].astype(jnp.float32)
    mixed = (picked * weights[None, :, :, None]).astype(jnp.bfloat16)
    pushed = jnp.einsum('rnkb,keb->rne', mixed.astype(jnp.float32), coupling.astype(jnp.float32))
    forced = (current.astype(jnp.float32) + pushed).astype(jnp.bfloat16)
    return jnp.einsum('ieq,riq->rie', inverse_table.astype(jnp.float32), forced.astype(jnp.float32)).astype(jnp.bfloat16)

def step_adjoint(current, inverse_table, coupling, weights, pattern):
    reached = jnp.einsum('ieq,rie->riq', inverse_table.astype(jnp.float32), current.astype(jnp.float32)).astype(jnp.bfloat16)
    pulled = jnp.einsum('rne,keb->rnkb', reached.astype(jnp.float32), coupling.astype(jnp.float32)).astype(jnp.bfloat16)
    terms = pulled.astype(jnp.float32) * weights[None, :, :, None]
    spread = jnp.zeros(reached.shape, jnp.float32).at[:, pattern, :].add(terms)
    return (reached.astype(jnp.float32) + spread).astype(jnp.bfloat16)

def reference(panel, seeds, inverses, coupling, weights, pattern, counts):
    current = panel.reshape(DIRS, NB, BLOCK)
    tangents = []
    for segment in range(SEGS):
        for step_index in range(STEPS_MAX):
            advanced = step_forward(current, inverses[segment], coupling[segment], weights, pattern)
            current = jnp.where(step_index < counts[segment], advanced, current)
        tangents.append(current)
    adjoints = [None] * SEGS
    carried = jnp.zeros((DIRS, NB, BLOCK), jnp.bfloat16)
    order_list = [(1 - round_index) % SEGS for round_index in range(SEGS)]
    for segment in order_list:
        current = (seeds[segment].reshape(DIRS, NB, BLOCK).astype(jnp.float32) + carried.astype(jnp.float32)).astype(jnp.bfloat16)
        for step_index in range(STEPS_MAX):
            advanced = step_adjoint(current, inverses[segment], coupling[segment], weights, pattern)
            current = jnp.where(step_index < counts[segment], advanced, current)
        adjoints[segment] = current
        carried = current
    projected = jnp.zeros((DIRS, DIRS), jnp.float32)
    for segment in range(SEGS):
        left_panel = adjoints[segment].reshape(DIRS, NS)
        right_panel = tangents[segment].reshape(DIRS, NS)
        projected = projected + jnp.dot(left_panel, right_panel.T, preferred_element_type=jnp.float32)
    projected = projected * (1.0 / math.sqrt(NS * SEGS))
    tangent = jnp.stack([item.reshape(DIRS, NS) for item in tangents])
    adjoint = jnp.stack([item.reshape(DIRS, NS) for item in adjoints])
    return (tangent, adjoint, projected)
```

```python
import math

import jax
import jax.numpy as jnp
from jax import lax
from jax.sharding import PartitionSpec as P


def shifted_ring(value, axis, steps):
    count = lax.axis_size(axis)
    pairs = [(source, (source + steps) % count) for source in range(count)]
    return lax.ppermute(value, axis, pairs)


def body(panel, seeds, inverses, coupling, weights, pattern, counts):
    blocks = pattern.shape[0]
    couple = pattern.shape[1]
    block_width = coupling.shape[-1]
    dir_count = panel.shape[0]
    start_panel = panel.reshape(dir_count, blocks, block_width)
    seed_panel = seeds[0].reshape(dir_count, blocks, block_width)
    coupling_here = coupling[0]
    seg_count = lax.axis_size("seg")
    position = lax.axis_index("seg")
    steps_here = counts[position]

    inverse_all = lax.all_gather(inverses[0], "dir", axis=0, tiled=True)

    flat_pattern = pattern.reshape(blocks * couple)
    flat_weights = weights.reshape(blocks * couple)
    picker = (flat_pattern[:, None] == jnp.arange(blocks, dtype=flat_pattern.dtype)[None, :])
    picker_bf = picker.astype(jnp.bfloat16)
    picker_f32 = picker.astype(jnp.float32)

    def step_forward(current):
        picked = jnp.einsum(
            "mj,rjb->rmb", picker_bf, current, preferred_element_type=jnp.float32
        )
        mixed = (picked * flat_weights[None, :, None]).astype(jnp.bfloat16)
        mixed = mixed.reshape(dir_count, blocks, couple, block_width)
        pushed = jnp.einsum(
            "rnkb,keb->rne", mixed, coupling_here, preferred_element_type=jnp.float32
        )
        forced = (current.astype(jnp.float32) + pushed).astype(jnp.bfloat16)
        return jnp.einsum(
            "ieq,riq->rie", inverse_all, forced, preferred_element_type=jnp.float32
        ).astype(jnp.bfloat16)

    def step_adjoint(current):
        reached = jnp.einsum(
            "ieq,rie->riq", inverse_all, current, preferred_element_type=jnp.float32
        ).astype(jnp.bfloat16)
        pulled = jnp.einsum(
            "rne,keb->rnkb", reached, coupling_here, preferred_element_type=jnp.float32
        ).astype(jnp.bfloat16)
        terms = pulled.reshape(dir_count, blocks * couple, block_width).astype(
            jnp.float32
        ) * flat_weights[None, :, None]
        spread = jnp.einsum(
            "mj,rmb->rjb",
            picker_f32,
            terms,
            preferred_element_type=jnp.float32,
            precision=lax.Precision.HIGHEST,
        )
        return (reached.astype(jnp.float32) + spread).astype(jnp.bfloat16)

    def run_steps(step, current):
        return lax.fori_loop(0, steps_here, lambda _, value: step(value), current)

    def round_body(round_index, state):
        forward_packet, adjoint_packet, tangent_out, adjoint_out = state
        forward_active = position == round_index
        adjoint_active = position == (1 - round_index + seg_count) % seg_count

        def forward_work(operands):
            packet, _ = operands
            advanced = run_steps(step_forward, packet)
            return advanced, advanced

        forward_packet, tangent_out = lax.cond(
            forward_active, forward_work, lambda operands: operands, (forward_packet, tangent_out)
        )

        def adjoint_work(operands):
            packet, _ = operands
            start_state = (
                seed_panel.astype(jnp.float32) + packet.astype(jnp.float32)
            ).astype(jnp.bfloat16)
            advanced = run_steps(step_adjoint, start_state)
            return advanced, advanced

        adjoint_packet, adjoint_out = lax.cond(
            adjoint_active, adjoint_work, lambda operands: operands, (adjoint_packet, adjoint_out)
        )
        forward_packet = shifted_ring(forward_packet, "seg", 1)
        adjoint_packet = shifted_ring(adjoint_packet, "seg", -1)
        return forward_packet, adjoint_packet, tangent_out, adjoint_out

    empty_panel = jnp.zeros_like(start_panel)
    state = (start_panel, empty_panel, empty_panel, empty_panel)
    state = lax.fori_loop(0, seg_count, round_body, state)
    tangent_flat = state[2].reshape(dir_count, blocks * block_width)
    adjoint_flat = state[3].reshape(dir_count, blocks * block_width)
    both = jnp.stack([tangent_flat, adjoint_flat])
    rows_both = lax.all_to_all(both, "dir", split_axis=2, concat_axis=1, tiled=True)
    rows_tangent, rows_adjoint = rows_both[0], rows_both[1]
    scale = 1.0 / math.sqrt(blocks * block_width * seg_count)
    partial_gram = (
        lax.dot_general(
            rows_adjoint, rows_tangent, (((1,), (1,)), ((), ())), preferred_element_type=jnp.float32
        )
        * scale
    )
    own_rows = lax.psum_scatter(partial_gram, "dir", scatter_dimension=0, tiled=True)
    projected = lax.psum(own_rows, "seg")
    return (tangent_flat[None], adjoint_flat[None], projected)


def solution(mesh):
    in_specs = (
        P("dir", None),
        P("seg", "dir", None),
        P("seg", "dir", None, None),
        P("seg", None, None, None),
        P(),
        P(),
        P(),
    )
    out_specs = (P("seg", "dir", None), P("seg", "dir", None), P("dir", None))
    return jax.shard_map(body, mesh=mesh, in_specs=in_specs, out_specs=out_specs, check_vma=False)
```

```python
import math

import jax
import jax.numpy as jnp
from jax import lax
from jax.sharding import PartitionSpec as P


def shifted_ring(value, axis, steps):
    count = lax.axis_size(axis)
    pairs = [(source, (source + steps) % count) for source in range(count)]
    return lax.ppermute(value, axis, pairs)


def body(panel, seeds, inverses, coupling, weights, pattern, counts):
    blocks = pattern.shape[0]
    couple = pattern.shape[1]
    block_width = coupling.shape[-1]
    dir_count = panel.shape[0]
    start_panel = panel.reshape(dir_count, blocks, block_width)
    seed_panel = seeds[0].reshape(dir_count, blocks, block_width)
    coupling_here = coupling[0]
    seg_count = lax.axis_size("seg")
    position = lax.axis_index("seg")
    steps_here = counts[position]

    dir_size = lax.axis_size("dir")
    dir_index = lax.axis_index("dir")
    parity = dir_index % 2
    parity_groups = [list(range(p, dir_size, 2)) for p in range(2)]
    half_table = lax.all_gather(
        inverses[0], "dir", axis=0, tiled=False, axis_index_groups=parity_groups
    )
    partner_pairs = [(d, d ^ 1) for d in range(dir_size)]
    other_table = lax.ppermute(half_table, "dir", partner_pairs)
    table_shape = (dir_size // 2, 2) + inverses.shape[1:]
    full_table = jnp.zeros(table_shape, inverses.dtype)
    full_table = lax.dynamic_update_index_in_dim(full_table, half_table, parity, 1)
    full_table = lax.dynamic_update_index_in_dim(full_table, other_table, 1 - parity, 1)
    inverse_all = full_table.reshape((blocks,) + inverses.shape[2:])

    flat_pattern = pattern.reshape(blocks * couple)
    flat_weights = weights.reshape(blocks * couple)
    picker = (flat_pattern[:, None] == jnp.arange(blocks, dtype=flat_pattern.dtype)[None, :])
    picker_bf = picker.astype(jnp.bfloat16)
    picker_f32 = picker.astype(jnp.float32)

    def step_forward(current):
        picked = jnp.einsum(
            "mj,rjb->rmb", picker_bf, current, preferred_element_type=jnp.float32
        )
        mixed = (picked * flat_weights[None, :, None]).astype(jnp.bfloat16)
        mixed = mixed.reshape(dir_count, blocks, couple, block_width)
        pushed = jnp.einsum(
            "rnkb,keb->rne", mixed, coupling_here, preferred_element_type=jnp.float32
        )
        forced = (current.astype(jnp.float32) + pushed).astype(jnp.bfloat16)
        return jnp.einsum(
            "ieq,riq->rie", inverse_all, forced, preferred_element_type=jnp.float32
        ).astype(jnp.bfloat16)

    def step_adjoint(current):
        reached = jnp.einsum(
            "ieq,rie->riq", inverse_all, current, preferred_element_type=jnp.float32
        ).astype(jnp.bfloat16)
        pulled = jnp.einsum(
            "rne,keb->rnkb", reached, coupling_here, preferred_element_type=jnp.float32
        ).astype(jnp.bfloat16)
        terms = pulled.reshape(dir_count, blocks * couple, block_width).astype(
            jnp.float32
        ) * flat_weights[None, :, None]
        spread = jnp.einsum(
            "mj,rmb->rjb",
            picker_f32,
            terms,
            preferred_element_type=jnp.float32,
            precision=lax.Precision.HIGHEST,
        )
        return (reached.astype(jnp.float32) + spread).astype(jnp.bfloat16)

    def run_steps(step, current):
        return lax.fori_loop(0, steps_here, lambda _, value: step(value), current)

    def round_body(round_index, state):
        forward_packet, adjoint_packet, tangent_out, adjoint_out = state
        forward_active = position == round_index
        adjoint_active = position == (1 - round_index + seg_count) % seg_count

        def forward_work(operands):
            packet, _ = operands
            advanced = run_steps(step_forward, packet)
            return advanced, advanced

        forward_packet, tangent_out = lax.cond(
            forward_active, forward_work, lambda operands: operands, (forward_packet, tangent_out)
        )

        def adjoint_work(operands):
            packet, _ = operands
            start_state = (
                seed_panel.astype(jnp.float32) + packet.astype(jnp.float32)
            ).astype(jnp.bfloat16)
            advanced = run_steps(step_adjoint, start_state)
            return advanced, advanced

        adjoint_packet, adjoint_out = lax.cond(
            adjoint_active, adjoint_work, lambda operands: operands, (adjoint_packet, adjoint_out)
        )
        forward_packet = shifted_ring(forward_packet, "seg", 1)
        adjoint_packet = shifted_ring(adjoint_packet, "seg", -1)
        return forward_packet, adjoint_packet, tangent_out, adjoint_out

    empty_panel = jnp.zeros_like(start_panel)
    state = (start_panel, empty_panel, empty_panel, empty_panel)
    state = lax.fori_loop(0, seg_count, round_body, state)
    tangent_state, adjoint_state = state[2], state[3]
    chunk_blocks = blocks // dir_size

    def dest_major(values):
        split = values.reshape(dir_count, dir_size, chunk_blocks, block_width)
        return jnp.transpose(split, (1, 0, 2, 3))

    both = jnp.concatenate([dest_major(tangent_state), dest_major(adjoint_state)], axis=1)
    rows_both = lax.all_to_all(both, "dir", split_axis=0, concat_axis=0, tiled=True)
    rows_tangent = rows_both[:, :dir_count]
    rows_adjoint = rows_both[:, dir_count:]
    scale = 1.0 / math.sqrt(blocks * block_width * seg_count)
    partial_gram = jnp.einsum(
        "jrbl,kqbl->jrkq", rows_adjoint, rows_tangent, preferred_element_type=jnp.float32
    ).reshape(dir_size * dir_count, dir_size * dir_count) * scale
    full_gram = lax.psum(partial_gram, ("seg", "dir"))
    projected = lax.dynamic_slice_in_dim(full_gram, dir_index * dir_count, dir_count, 0)
    tangent_flat = tangent_state.reshape(dir_count, blocks * block_width)
    adjoint_flat = adjoint_state.reshape(dir_count, blocks * block_width)
    return (tangent_flat[None], adjoint_flat[None], projected)


def solution(mesh):
    in_specs = (
        P("dir", None),
        P("seg", "dir", None),
        P("seg", "dir", None, None),
        P("seg", None, None, None),
        P(),
        P(),
        P(),
    )
    out_specs = (P("seg", "dir", None), P("seg", "dir", None), P("dir", None))
    return jax.shard_map(body, mesh=mesh, in_specs=in_specs, out_specs=out_specs, check_vma=False)
```

```python
import math

import jax
import jax.numpy as jnp
from jax import lax
from jax.sharding import PartitionSpec as P


def shifted_ring(value, axis, steps):
    count = lax.axis_size(axis)
    pairs = [(source, (source + steps) % count) for source in range(count)]
    return lax.ppermute(value, axis, pairs)


def body(panel, seeds, inverses, coupling, weights, pattern, counts):
    blocks = pattern.shape[0]
    couple = pattern.shape[1]
    block_width = coupling.shape[-1]
    dir_count = panel.shape[0]
    start_panel = panel.reshape(dir_count, blocks, block_width)
    seed_panel = seeds[0].reshape(dir_count, blocks, block_width)
    coupling_here = coupling[0]
    seg_count = lax.axis_size("seg")
    position = lax.axis_index("seg")
    steps_here = counts[position]

    dir_size = lax.axis_size("dir")
    dir_index = lax.axis_index("dir")
    inverse_all = lax.all_gather(inverses[0], "dir", axis=0, tiled=True)

    flat_pattern = pattern.reshape(blocks * couple)
    flat_weights = weights.reshape(blocks * couple)
    picker = (flat_pattern[:, None] == jnp.arange(blocks, dtype=flat_pattern.dtype)[None, :])
    picker_bf = picker.astype(jnp.bfloat16)
    picker_f32 = picker.astype(jnp.float32)

    def step_forward(current):
        picked = jnp.einsum(
            "mj,rjb->rmb", picker_bf, current, preferred_element_type=jnp.float32
        )
        mixed = (picked * flat_weights[None, :, None]).astype(jnp.bfloat16)
        mixed = mixed.reshape(dir_count, blocks, couple, block_width)
        pushed = jnp.einsum(
            "rnkb,keb->rne", mixed, coupling_here, preferred_element_type=jnp.float32
        )
        forced = (current.astype(jnp.float32) + pushed).astype(jnp.bfloat16)
        return jnp.einsum(
            "ieq,riq->rie", inverse_all, forced, preferred_element_type=jnp.float32
        ).astype(jnp.bfloat16)

    def step_adjoint(current):
        reached = jnp.einsum(
            "ieq,rie->riq", inverse_all, current, preferred_element_type=jnp.float32
        ).astype(jnp.bfloat16)
        pulled = jnp.einsum(
            "rne,keb->rnkb", reached, coupling_here, preferred_element_type=jnp.float32
        ).astype(jnp.bfloat16)
        terms = pulled.reshape(dir_count, blocks * couple, block_width).astype(
            jnp.float32
        ) * flat_weights[None, :, None]
        spread = jnp.einsum(
            "mj,rmb->rjb",
            picker_f32,
            terms,
            preferred_element_type=jnp.float32,
            precision=lax.Precision.HIGHEST,
        )
        return (reached.astype(jnp.float32) + spread).astype(jnp.bfloat16)

    def run_steps(step, current):
        return lax.fori_loop(0, steps_here, lambda _, value: step(value), current)

    def forward_work(state):
        forward_packet, adjoint_packet, tangent_out, adjoint_out = state
        advanced = run_steps(step_forward, forward_packet)
        return advanced, adjoint_packet, advanced, adjoint_out

    def adjoint_work(state):
        forward_packet, adjoint_packet, tangent_out, adjoint_out = state
        start_state = (
            seed_panel.astype(jnp.float32) + adjoint_packet.astype(jnp.float32)
        ).astype(jnp.bfloat16)
        advanced = run_steps(step_adjoint, start_state)
        return forward_packet, advanced, tangent_out, advanced

    def compute_round(round_index, state):
        forward_active = position == round_index
        adjoint_active = position == (1 - round_index + seg_count) % seg_count
        branch = jnp.where(forward_active, 1, jnp.where(adjoint_active, 2, 0))
        return lax.switch(branch, [lambda s: s, forward_work, adjoint_work], state)

    def round_body(round_index, state):
        forward_packet, adjoint_packet, tangent_out, adjoint_out = compute_round(
            round_index, state
        )
        forward_packet = shifted_ring(forward_packet, "seg", 1)
        adjoint_packet = shifted_ring(adjoint_packet, "seg", -1)
        return forward_packet, adjoint_packet, tangent_out, adjoint_out

    empty_panel = jnp.zeros_like(start_panel)
    state = (start_panel, empty_panel, empty_panel, empty_panel)
    state = lax.fori_loop(0, seg_count - 1, round_body, state)
    state = compute_round(seg_count - 1, state)
    tangent_state, adjoint_state = state[2], state[3]
    chunk_blocks = blocks // dir_size

    def dest_major(values):
        split = values.reshape(dir_count, dir_size, chunk_blocks, block_width)
        return jnp.transpose(split, (1, 0, 2, 3))

    both = jnp.concatenate([dest_major(tangent_state), dest_major(adjoint_state)], axis=1)
    rows_both = lax.all_to_all(both, "dir", split_axis=0, concat_axis=0, tiled=True)
    rows_tangent = rows_both[:, :dir_count]
    rows_adjoint = rows_both[:, dir_count:]
    scale = 1.0 / math.sqrt(blocks * block_width * seg_count)
    partial_gram = jnp.einsum(
        "jrbl,kqbl->jrkq", rows_adjoint, rows_tangent, preferred_element_type=jnp.float32
    ).reshape(dir_size * dir_count, dir_size * dir_count) * scale
    by_owner = partial_gram.reshape(dir_size, dir_count, dir_size * dir_count)
    from_chunks = lax.all_to_all(by_owner, "dir", split_axis=0, concat_axis=0, tiled=True)
    projected = lax.psum(jnp.sum(from_chunks, axis=0), "seg")
    tangent_flat = tangent_state.reshape(dir_count, blocks * block_width)
    adjoint_flat = adjoint_state.reshape(dir_count, blocks * block_width)
    return (tangent_flat[None], adjoint_flat[None], projected)


def solution(mesh):
    in_specs = (
        P("dir", None),
        P("seg", "dir", None),
        P("seg", "dir", None, None),
        P("seg", None, None, None),
        P(),
        P(),
        P(),
    )
    out_specs = (P("seg", "dir", None), P("seg", "dir", None), P("dir", None))
    return jax.shard_map(body, mesh=mesh, in_specs=in_specs, out_specs=out_specs, check_vma=False)
```

```python
import math

import jax
import jax.numpy as jnp
from jax import lax
from jax.sharding import PartitionSpec as P


def shifted_ring(value, axis, steps):
    count = lax.axis_size(axis)
    pairs = [(source, (source + steps) % count) for source in range(count)]
    return lax.ppermute(value, axis, pairs)


def body(panel, seeds, inverses, coupling, weights, pattern, counts):
    blocks = pattern.shape[0]
    couple = pattern.shape[1]
    block_width = coupling.shape[-1]
    dir_count = panel.shape[0]

    def block_major(values):
        return jnp.transpose(values.reshape(dir_count, blocks, block_width), (1, 0, 2))

    def dir_major(values):
        return jnp.transpose(values, (1, 0, 2)).reshape(dir_count, blocks * block_width)

    start_panel = block_major(panel)
    seed_panel = block_major(seeds[0])
    coupling_here = coupling[0]
    seg_count = lax.axis_size("seg")
    position = lax.axis_index("seg")
    steps_here = counts[position]
    dir_size = lax.axis_size("dir")

    inverse_all = lax.all_gather(inverses[0], "dir", axis=0, tiled=True)
    inverse_all_t = jnp.transpose(inverse_all, (0, 2, 1))

    pattern_ki = jnp.transpose(pattern).reshape(couple * blocks)
    weights_ki = jnp.transpose(weights).reshape(couple * blocks)
    picker = pattern_ki[:, None] == jnp.arange(blocks, dtype=pattern_ki.dtype)[None, :]
    picker_bf = picker.astype(jnp.bfloat16)
    picker_f32 = picker.astype(jnp.float32)

    def step_forward(current):
        picked = jnp.einsum(
            "mj,jrb->mrb", picker_bf, current, preferred_element_type=jnp.float32
        )
        mixed = (picked * weights_ki[:, None, None]).astype(jnp.bfloat16)
        mixed = mixed.reshape(couple, blocks, dir_count, block_width)
        pushed = current.astype(jnp.float32)
        for k in range(couple):
            pushed = pushed + jnp.einsum(
                "nrb,eb->nre", mixed[k], coupling_here[k], preferred_element_type=jnp.float32
            )
        forced = pushed.astype(jnp.bfloat16)
        return jnp.einsum(
            "iqe,irq->ire", inverse_all_t, forced, preferred_element_type=jnp.float32
        ).astype(jnp.bfloat16)

    def step_adjoint(current):
        reached = jnp.einsum(
            "ieq,ire->irq", inverse_all, current, preferred_element_type=jnp.float32
        ).astype(jnp.bfloat16)
        pulled = jnp.stack(
            [
                jnp.einsum(
                    "nre,eb->nrb", reached, coupling_here[k], preferred_element_type=jnp.float32
                ).astype(jnp.bfloat16)
                for k in range(couple)
            ]
        ).reshape(couple * blocks, dir_count, block_width)
        terms = pulled.astype(jnp.float32) * weights_ki[:, None, None]
        spread = jnp.einsum(
            "mj,mrb->jrb",
            picker_f32,
            terms,
            preferred_element_type=jnp.float32,
            precision=lax.Precision.HIGHEST,
        )
        return (reached.astype(jnp.float32) + spread).astype(jnp.bfloat16)

    def run_steps(step, current):
        return lax.fori_loop(0, steps_here, lambda _, value: step(value), current)

    def forward_work(state):
        forward_packet, adjoint_packet, tangent_out, adjoint_out = state
        advanced = run_steps(step_forward, forward_packet)
        return advanced, adjoint_packet, advanced, adjoint_out

    def adjoint_work(state):
        forward_packet, adjoint_packet, tangent_out, adjoint_out = state
        start_state = (
            seed_panel.astype(jnp.float32) + adjoint_packet.astype(jnp.float32)
        ).astype(jnp.bfloat16)
        advanced = run_steps(step_adjoint, start_state)
        return forward_packet, advanced, tangent_out, advanced

    def compute_round(round_index, state):
        forward_active = position == round_index
        adjoint_active = position == (1 - round_index + seg_count) % seg_count
        branch = jnp.where(forward_active, 1, jnp.where(adjoint_active, 2, 0))
        return lax.switch(branch, [lambda s: s, forward_work, adjoint_work], state)

    def round_body(round_index, state):
        forward_packet, adjoint_packet, tangent_out, adjoint_out = compute_round(
            round_index, state
        )
        forward_packet = shifted_ring(forward_packet, "seg", 1)
        adjoint_packet = shifted_ring(adjoint_packet, "seg", -1)
        return forward_packet, adjoint_packet, tangent_out, adjoint_out

    empty_panel = jnp.zeros_like(start_panel)
    state = (start_panel, empty_panel, empty_panel, empty_panel)
    state = lax.fori_loop(0, seg_count - 1, round_body, state)
    state = compute_round(seg_count - 1, state)
    tangent_state, adjoint_state = state[2], state[3]
    chunk_blocks = blocks // dir_size

    both = jnp.stack(
        [
            tangent_state.reshape(dir_size, chunk_blocks, dir_count, block_width),
            adjoint_state.reshape(dir_size, chunk_blocks, dir_count, block_width),
        ],
        axis=1,
    )
    rows_both = lax.all_to_all(both, "dir", split_axis=0, concat_axis=0, tiled=True)
    rows_tangent = rows_both[:, 0]
    rows_adjoint = rows_both[:, 1]
    scale = 1.0 / math.sqrt(blocks * block_width * seg_count)
    partial_gram = jnp.einsum(
        "jbrl,kbql->jrkq", rows_adjoint, rows_tangent, preferred_element_type=jnp.float32
    ).reshape(dir_size * dir_count, dir_size * dir_count) * scale
    by_owner = partial_gram.reshape(dir_size, dir_count, dir_size * dir_count)
    from_chunks = lax.all_to_all(by_owner, "dir", split_axis=0, concat_axis=0, tiled=True)
    projected = lax.psum(jnp.sum(from_chunks, axis=0), "seg")
    return (dir_major(tangent_state)[None], dir_major(adjoint_state)[None], projected)


def solution(mesh):
    in_specs = (
        P("dir", None),
        P("seg", "dir", None),
        P("seg", "dir", None, None),
        P("seg", None, None, None),
        P(),
        P(),
        P(),
    )
    out_specs = (P("seg", "dir", None), P("seg", "dir", None), P("dir", None))
    return jax.shard_map(body, mesh=mesh, in_specs=in_specs, out_specs=out_specs, check_vma=False)
```

```python
import math

import jax
import jax.numpy as jnp
from jax import lax
from jax.sharding import PartitionSpec as P


def shifted_ring(value, axis, steps):
    count = lax.axis_size(axis)
    pairs = [(source, (source + steps) % count) for source in range(count)]
    return lax.ppermute(value, axis, pairs)


def body(panel, seeds, inverses, coupling, weights, pattern, counts):
    blocks = pattern.shape[0]
    couple = pattern.shape[1]
    block_width = coupling.shape[-1]
    dir_count = panel.shape[0]

    def block_major(values):
        return jnp.transpose(values.reshape(dir_count, blocks, block_width), (1, 0, 2))

    def dir_major(values):
        return jnp.transpose(values, (1, 0, 2)).reshape(dir_count, blocks * block_width)

    start_panel = block_major(panel)
    seed_panel = block_major(seeds[0])
    coupling_here = coupling[0]
    seg_count = lax.axis_size("seg")
    position = lax.axis_index("seg")
    steps_here = counts[position]
    dir_size = lax.axis_size("dir")

    inverse_all = lax.all_gather(inverses[0], "dir", axis=0, tiled=True)

    pattern_ki = jnp.transpose(pattern).reshape(couple * blocks)
    weights_ki = jnp.transpose(weights).reshape(couple * blocks)
    picker = pattern_ki[:, None] == jnp.arange(blocks, dtype=pattern_ki.dtype)[None, :]
    picker_bf = picker.astype(jnp.bfloat16)
    picker_f32 = picker.astype(jnp.float32)

    def step_forward(current, table, transposed):
        picked = jnp.einsum(
            "mj,jrb->mrb", picker_bf, current, preferred_element_type=jnp.float32
        )
        mixed = (picked * weights_ki[:, None, None]).astype(jnp.bfloat16)
        mixed = mixed.reshape(couple, blocks, dir_count, block_width)
        pushed = current.astype(jnp.float32)
        for k in range(couple):
            pushed = pushed + jnp.einsum(
                "nrb,eb->nre", mixed[k], coupling_here[k], preferred_element_type=jnp.float32
            )
        forced = pushed.astype(jnp.bfloat16)
        spec = "iqe,irq->ire" if transposed else "ieq,irq->ire"
        return jnp.einsum(spec, table, forced, preferred_element_type=jnp.float32).astype(
            jnp.bfloat16
        )

    def step_adjoint(current):
        reached = jnp.einsum(
            "ieq,ire->irq", inverse_all, current, preferred_element_type=jnp.float32
        ).astype(jnp.bfloat16)
        pulled = jnp.stack(
            [
                jnp.einsum(
                    "nre,eb->nrb", reached, coupling_here[k], preferred_element_type=jnp.float32
                ).astype(jnp.bfloat16)
                for k in range(couple)
            ]
        ).reshape(couple * blocks, dir_count, block_width)
        terms = pulled.astype(jnp.float32) * weights_ki[:, None, None]
        spread = jnp.einsum(
            "mj,mrb->jrb",
            picker_f32,
            terms,
            preferred_element_type=jnp.float32,
            precision=lax.Precision.HIGHEST,
        )
        return (reached.astype(jnp.float32) + spread).astype(jnp.bfloat16)

    def run_steps(step, current):
        return lax.fori_loop(0, steps_here, lambda _, value: step(value), current)

    def forward_work(transposed, table_t, panels):
        forward_packet, adjoint_packet, tangent_out, adjoint_out = panels
        table = table_t if transposed else inverse_all
        advanced = run_steps(lambda value: step_forward(value, table, transposed), forward_packet)
        return advanced, adjoint_packet, advanced, adjoint_out

    def adjoint_work(panels):
        forward_packet, adjoint_packet, tangent_out, adjoint_out = panels
        start_state = (
            seed_panel.astype(jnp.float32) + adjoint_packet.astype(jnp.float32)
        ).astype(jnp.bfloat16)
        advanced = run_steps(step_adjoint, start_state)
        return forward_packet, advanced, tangent_out, advanced

    def round_branch(round_index):
        forward_active = position == round_index
        adjoint_active = position == (1 - round_index + seg_count) % seg_count
        return jnp.where(forward_active, 1, jnp.where(adjoint_active, 2, 0))

    def pass_packets(panels):
        forward_packet, adjoint_packet, tangent_out, adjoint_out = panels
        forward_packet = shifted_ring(forward_packet, "seg", 1)
        adjoint_packet = shifted_ring(adjoint_packet, "seg", -1)
        return forward_packet, adjoint_packet, tangent_out, adjoint_out

    empty_panel = jnp.zeros_like(start_panel)
    panels = (start_panel, empty_panel, empty_panel, empty_panel)

    def round0_idle(panels):
        return panels, jnp.transpose(inverse_all, (0, 2, 1))

    def round0_forward(panels):
        return forward_work(False, None, panels), jnp.zeros_like(inverse_all)

    def round0_adjoint(panels):
        return adjoint_work(panels), jnp.zeros_like(inverse_all)

    panels, table_t = lax.switch(
        round_branch(0), [round0_idle, round0_forward, round0_adjoint], panels
    )
    panels = pass_packets(panels)

    def round_body(round_index, panels):
        def forward_either(panels):
            return lax.cond(
                round_index < 2,
                lambda p: forward_work(False, None, p),
                lambda p: forward_work(True, table_t, p),
                panels,
            )

        panels = lax.switch(
            round_branch(round_index), [lambda p: p, forward_either, adjoint_work], panels
        )
        return pass_packets(panels)

    state = lax.fori_loop(1, seg_count, round_body, panels)
    tangent_state, adjoint_state = state[2], state[3]
    chunk_blocks = blocks // dir_size

    both = jnp.stack(
        [
            tangent_state.reshape(dir_size, chunk_blocks, dir_count, block_width),
            adjoint_state.reshape(dir_size, chunk_blocks, dir_count, block_width),
        ],
        axis=1,
    )
    rows_both = lax.all_to_all(both, "dir", split_axis=0, concat_axis=0, tiled=True)
    rows_tangent = rows_both[:, 0]
    rows_adjoint = rows_both[:, 1]
    scale = 1.0 / math.sqrt(blocks * block_width * seg_count)
    partial_gram = jnp.einsum(
        "jbrl,kbql->jrkq", rows_adjoint, rows_tangent, preferred_element_type=jnp.float32
    ).reshape(dir_size * dir_count, dir_size * dir_count) * scale
    by_owner = partial_gram.reshape(dir_size, dir_count, dir_size * dir_count)
    from_chunks = lax.all_to_all(by_owner, "dir", split_axis=0, concat_axis=0, tiled=True)
    projected = lax.psum(jnp.sum(from_chunks, axis=0), "seg")
    return (dir_major(tangent_state)[None], dir_major(adjoint_state)[None], projected)


def solution(mesh):
    in_specs = (
        P("dir", None),
        P("seg", "dir", None),
        P("seg", "dir", None, None),
        P("seg", None, None, None),
        P(),
        P(),
        P(),
    )
    out_specs = (P("seg", "dir", None), P("seg", "dir", None), P("dir", None))
    return jax.shard_map(body, mesh=mesh, in_specs=in_specs, out_specs=out_specs, check_vma=False)
```

```python
import math

import jax
import jax.numpy as jnp
from jax import lax
from jax.sharding import PartitionSpec as P


def shifted_ring(value, axis, steps):
    count = lax.axis_size(axis)
    pairs = [(source, (source + steps) % count) for source in range(count)]
    return lax.ppermute(value, axis, pairs)


def body(panel, seeds, inverses, coupling, weights, pattern, counts):
    blocks = pattern.shape[0]
    couple = pattern.shape[1]
    block_width = coupling.shape[-1]
    dir_count = panel.shape[0]

    def block_major(values):
        return jnp.transpose(values.reshape(dir_count, blocks, block_width), (1, 0, 2))

    def dir_major(values):
        return jnp.transpose(values, (1, 0, 2)).reshape(dir_count, blocks * block_width)

    start_panel = block_major(panel)
    seed_panel = block_major(seeds[0])
    coupling_here = coupling[0]
    seg_count = lax.axis_size("seg")
    position = lax.axis_index("seg")
    steps_here = counts[position]
    dir_size = lax.axis_size("dir")

    inverse_all = lax.all_gather(inverses[0], "dir", axis=0, tiled=True)
    inverse_all_t = jnp.transpose(inverse_all, (0, 2, 1))

    pattern_ki = jnp.transpose(pattern).reshape(couple * blocks)
    weights_ki = jnp.transpose(weights).reshape(couple * blocks)
    picker = pattern_ki[:, None] == jnp.arange(blocks, dtype=pattern_ki.dtype)[None, :]
    picker_bf = picker.astype(jnp.bfloat16)
    picker_f32 = picker.astype(jnp.float32)

    def step_forward(current):
        picked = jnp.einsum(
            "mj,jrb->mrb", picker_bf, current, preferred_element_type=jnp.float32
        )
        mixed = (picked * weights_ki[:, None, None]).astype(jnp.bfloat16)
        mixed = mixed.reshape(couple, blocks, dir_count, block_width)
        pushed = current.astype(jnp.float32)
        for k in range(couple):
            pushed = pushed + jnp.einsum(
                "nrb,eb->nre", mixed[k], coupling_here[k], preferred_element_type=jnp.float32
            )
        forced = pushed.astype(jnp.bfloat16)
        return jnp.einsum(
            "iqe,irq->ire", inverse_all_t, forced, preferred_element_type=jnp.float32
        ).astype(jnp.bfloat16)

    def step_adjoint(current):
        reached = jnp.einsum(
            "ieq,ire->irq", inverse_all, current, preferred_element_type=jnp.float32
        ).astype(jnp.bfloat16)
        pulled = jnp.stack(
            [
                jnp.einsum(
                    "nre,eb->nrb", reached, coupling_here[k], preferred_element_type=jnp.float32
                ).astype(jnp.bfloat16)
                for k in range(couple)
            ]
        ).reshape(couple * blocks, dir_count, block_width)
        terms = pulled.astype(jnp.float32) * weights_ki[:, None, None]
        spread = jnp.einsum(
            "mj,mrb->jrb",
            picker_f32,
            terms,
            preferred_element_type=jnp.float32,
            precision=lax.Precision.HIGHEST,
        )
        return (reached.astype(jnp.float32) + spread).astype(jnp.bfloat16)

    def run_steps(step, current):
        return lax.fori_loop(0, steps_here, lambda _, value: step(value), current)

    def forward_work(state):
        forward_packet, adjoint_packet, tangent_out, adjoint_out = state
        advanced = run_steps(step_forward, forward_packet)
        return advanced, adjoint_packet, advanced, adjoint_out

    def adjoint_work(state):
        forward_packet, adjoint_packet, tangent_out, adjoint_out = state
        start_state = (
            seed_panel.astype(jnp.float32) + adjoint_packet.astype(jnp.float32)
        ).astype(jnp.bfloat16)
        advanced = run_steps(step_adjoint, start_state)
        return forward_packet, advanced, tangent_out, advanced

    def compute_round(round_index, state):
        forward_active = position == round_index
        adjoint_active = position == (1 - round_index + seg_count) % seg_count
        branch = jnp.where(forward_active, 1, jnp.where(adjoint_active, 2, 0))
        return lax.switch(branch, [lambda s: s, forward_work, adjoint_work], state)

    def round_body(round_index, state):
        forward_packet, adjoint_packet, tangent_out, adjoint_out = compute_round(
            round_index, state
        )
        forward_packet = shifted_ring(forward_packet, "seg", 1)
        adjoint_packet = shifted_ring(adjoint_packet, "seg", -1)
        return forward_packet, adjoint_packet, tangent_out, adjoint_out

    empty_panel = jnp.zeros_like(start_panel)
    state = (start_panel, empty_panel, empty_panel, empty_panel)
    state = lax.fori_loop(0, seg_count, round_body, state)
    tangent_state, adjoint_state = state[2], state[3]
    chunk_blocks = blocks // dir_size

    both = jnp.stack(
        [
            tangent_state.reshape(dir_size, chunk_blocks, dir_count, block_width),
            adjoint_state.reshape(dir_size, chunk_blocks, dir_count, block_width),
        ],
        axis=1,
    )
    rows_both = lax.all_to_all(both, "dir", split_axis=0, concat_axis=0, tiled=True)
    rows_tangent = rows_both[:, 0]
    rows_adjoint = rows_both[:, 1]
    scale = 1.0 / math.sqrt(blocks * block_width * seg_count)
    partial_gram = jnp.einsum(
        "jbrl,kbql->jrkq", rows_adjoint, rows_tangent, preferred_element_type=jnp.float32
    ).reshape(dir_size * dir_count, dir_size * dir_count) * scale
    by_owner = partial_gram.reshape(dir_size, dir_count, dir_size * dir_count)
    from_chunks = lax.all_to_all(by_owner, "dir", split_axis=0, concat_axis=0, tiled=True)
    projected = lax.psum(jnp.sum(from_chunks, axis=0), "seg")
    return (dir_major(tangent_state)[None], dir_major(adjoint_state)[None], projected)


def solution(mesh):
    in_specs = (
        P("dir", None),
        P("seg", "dir", None),
        P("seg", "dir", None, None),
        P("seg", None, None, None),
        P(),
        P(),
        P(),
    )
    out_specs = (P("seg", "dir", None), P("seg", "dir", None), P("dir", None))
    return jax.shard_map(body, mesh=mesh, in_specs=in_specs, out_specs=out_specs, check_vma=False)
```

```python
import math

import jax
import jax.numpy as jnp
from jax import lax
from jax.sharding import PartitionSpec as P


def shifted_ring(value, axis, steps):
    count = lax.axis_size(axis)
    pairs = [(source, (source + steps) % count) for source in range(count)]
    return lax.ppermute(value, axis, pairs)


def body(panel, seeds, inverses, coupling, weights, pattern, counts):
    blocks = pattern.shape[0]
    couple = pattern.shape[1]
    block_width = coupling.shape[-1]
    dir_count = panel.shape[0]

    def block_major(values):
        return jnp.transpose(values.reshape(dir_count, blocks, block_width), (1, 0, 2))

    def dir_major(values):
        return jnp.transpose(values, (1, 0, 2)).reshape(dir_count, blocks * block_width)

    start_panel = block_major(panel)
    seed_panel = block_major(seeds[0])
    coupling_here = coupling[0]
    seg_count = lax.axis_size("seg")
    position = lax.axis_index("seg")
    steps_here = counts[position]
    dir_size = lax.axis_size("dir")

    inverse_all = lax.all_gather(inverses[0], "dir", axis=0, tiled=True)
    inverse_all_t = jnp.transpose(inverse_all, (0, 2, 1))

    pattern_ki = jnp.transpose(pattern).reshape(couple * blocks)
    weights_ki = jnp.transpose(weights).reshape(couple * blocks)
    picker = pattern_ki[:, None] == jnp.arange(blocks, dtype=pattern_ki.dtype)[None, :]
    picker_bf = picker.astype(jnp.bfloat16)

    def step_forward(current):
        picked = jnp.einsum(
            "mj,jrb->mrb", picker_bf, current, preferred_element_type=jnp.float32
        )
        mixed = (picked * weights_ki[:, None, None]).astype(jnp.bfloat16)
        mixed = mixed.reshape(couple, blocks, dir_count, block_width)
        pushed = current.astype(jnp.float32)
        for k in range(couple):
            pushed = pushed + jnp.einsum(
                "nrb,eb->nre", mixed[k], coupling_here[k], preferred_element_type=jnp.float32
            )
        forced = pushed.astype(jnp.bfloat16)
        return jnp.einsum(
            "iqe,irq->ire", inverse_all_t, forced, preferred_element_type=jnp.float32
        ).astype(jnp.bfloat16)

    def step_adjoint(current):
        reached = jnp.einsum(
            "ieq,ire->irq", inverse_all, current, preferred_element_type=jnp.float32
        ).astype(jnp.bfloat16)
        pulled = jnp.stack(
            [
                jnp.einsum(
                    "nre,eb->nrb", reached, coupling_here[k], preferred_element_type=jnp.float32
                ).astype(jnp.bfloat16)
                for k in range(couple)
            ]
        ).reshape(couple * blocks, dir_count, block_width)
        terms = pulled.astype(jnp.float32) * weights_ki[:, None, None]
        terms_hi = terms.astype(jnp.bfloat16)
        terms_lo = (terms - terms_hi.astype(jnp.float32)).astype(jnp.bfloat16)
        spread = jnp.einsum(
            "mj,mrb->jrb", picker_bf, terms_hi, preferred_element_type=jnp.float32
        ) + jnp.einsum("mj,mrb->jrb", picker_bf, terms_lo, preferred_element_type=jnp.float32)
        return (reached.astype(jnp.float32) + spread).astype(jnp.bfloat16)

    def run_steps(step, current):
        return lax.fori_loop(0, steps_here, lambda _, value: step(value), current)

    def forward_work(state):
        forward_packet, adjoint_packet, tangent_out, adjoint_out = state
        advanced = run_steps(step_forward, forward_packet)
        return advanced, adjoint_packet, advanced, adjoint_out

    def adjoint_work(state):
        forward_packet, adjoint_packet, tangent_out, adjoint_out = state
        start_state = (
            seed_panel.astype(jnp.float32) + adjoint_packet.astype(jnp.float32)
        ).astype(jnp.bfloat16)
        advanced = run_steps(step_adjoint, start_state)
        return forward_packet, advanced, tangent_out, advanced

    def compute_round(round_index, state):
        forward_active = position == round_index
        adjoint_active = position == (1 - round_index + seg_count) % seg_count
        branch = jnp.where(forward_active, 1, jnp.where(adjoint_active, 2, 0))
        return lax.switch(branch, [lambda s: s, forward_work, adjoint_work], state)

    def round_body(round_index, state):
        forward_packet, adjoint_packet, tangent_out, adjoint_out = compute_round(
            round_index, state
        )
        forward_packet = shifted_ring(forward_packet, "seg", 1)
        adjoint_packet = shifted_ring(adjoint_packet, "seg", -1)
        return forward_packet, adjoint_packet, tangent_out, adjoint_out

    empty_panel = jnp.zeros_like(start_panel)
    state = (start_panel, empty_panel, empty_panel, empty_panel)
    state = lax.fori_loop(0, seg_count, round_body, state)
    tangent_state, adjoint_state = state[2], state[3]
    chunk_blocks = blocks // dir_size

    both = jnp.stack(
        [
            tangent_state.reshape(dir_size, chunk_blocks, dir_count, block_width),
            adjoint_state.reshape(dir_size, chunk_blocks, dir_count, block_width),
        ],
        axis=1,
    )
    rows_both = lax.all_to_all(both, "dir", split_axis=0, concat_axis=0, tiled=True)
    rows_tangent = rows_both[:, 0]
    rows_adjoint = rows_both[:, 1]
    scale = 1.0 / math.sqrt(blocks * block_width * seg_count)
    partial_gram = jnp.einsum(
        "jbrl,kbql->jrkq", rows_adjoint, rows_tangent, preferred_element_type=jnp.float32
    ).reshape(dir_size * dir_count, dir_size * dir_count) * scale
    full_gram = lax.psum(partial_gram, ("seg", "dir"))
    projected = lax.dynamic_slice_in_dim(full_gram, lax.axis_index("dir") * dir_count, dir_count, 0)
    return (dir_major(tangent_state)[None], dir_major(adjoint_state)[None], projected)


def solution(mesh):
    in_specs = (
        P("dir", None),
        P("seg", "dir", None),
        P("seg", "dir", None, None),
        P("seg", None, None, None),
        P(),
        P(),
        P(),
    )
    out_specs = (P("seg", "dir", None), P("seg", "dir", None), P("dir", None))
    return jax.shard_map(body, mesh=mesh, in_specs=in_specs, out_specs=out_specs, check_vma=False)
```

```python
import math

import jax
import jax.numpy as jnp
from jax import lax
from jax.sharding import PartitionSpec as P


def shifted_ring(value, axis, steps):
    count = lax.axis_size(axis)
    pairs = [(source, (source + steps) % count) for source in range(count)]
    return lax.ppermute(value, axis, pairs)


def body(panel, seeds, inverses, coupling, weights, pattern, counts):
    blocks = pattern.shape[0]
    couple = pattern.shape[1]
    block_width = coupling.shape[-1]
    dir_count = panel.shape[0]

    def block_major(values):
        return jnp.transpose(values.reshape(dir_count, blocks, block_width), (1, 0, 2))

    def dir_major(values):
        return jnp.transpose(values, (1, 0, 2)).reshape(dir_count, blocks * block_width)

    start_panel = block_major(panel)
    seed_panel = block_major(seeds[0])
    coupling_here = coupling[0]
    seg_count = lax.axis_size("seg")
    position = lax.axis_index("seg")
    steps_here = counts[position]
    dir_size = lax.axis_size("dir")

    inverse_all = lax.all_gather(inverses[0], "dir", axis=0, tiled=True)
    inverse_all_t = jnp.transpose(inverse_all, (0, 2, 1))

    pattern_ki = jnp.transpose(pattern).reshape(couple * blocks)
    weights_ki = jnp.transpose(weights).reshape(couple * blocks)
    picker = pattern_ki[:, None] == jnp.arange(blocks, dtype=pattern_ki.dtype)[None, :]
    picker_bf = picker.astype(jnp.bfloat16)

    def step_forward(current):
        picked = jnp.einsum(
            "mj,jrb->mrb", picker_bf, current, preferred_element_type=jnp.float32
        )
        mixed = (picked * weights_ki[:, None, None]).astype(jnp.bfloat16)
        mixed = mixed.reshape(couple, blocks, dir_count, block_width)
        pushed = current.astype(jnp.float32)
        for k in range(couple):
            pushed = pushed + jnp.einsum(
                "nrb,eb->nre", mixed[k], coupling_here[k], preferred_element_type=jnp.float32
            )
        forced = pushed.astype(jnp.bfloat16)
        return jnp.einsum(
            "iqe,irq->ire", inverse_all_t, forced, preferred_element_type=jnp.float32
        ).astype(jnp.bfloat16)

    def step_adjoint(current):
        reached = jnp.einsum(
            "ieq,ire->irq", inverse_all, current, preferred_element_type=jnp.float32
        ).astype(jnp.bfloat16)
        pulled = jnp.stack(
            [
                jnp.einsum(
                    "nre,eb->nrb", reached, coupling_here[k], preferred_element_type=jnp.float32
                ).astype(jnp.bfloat16)
                for k in range(couple)
            ]
        ).reshape(couple * blocks, dir_count, block_width)
        terms = pulled.astype(jnp.float32) * weights_ki[:, None, None]
        terms_hi = terms.astype(jnp.bfloat16)
        terms_lo = (terms - terms_hi.astype(jnp.float32)).astype(jnp.bfloat16)
        spread = jnp.einsum(
            "mj,mrb->jrb", picker_bf, terms_hi, preferred_element_type=jnp.float32
        ) + jnp.einsum("mj,mrb->jrb", picker_bf, terms_lo, preferred_element_type=jnp.float32)
        return (reached.astype(jnp.float32) + spread).astype(jnp.bfloat16)

    def run_steps(step, current):
        return lax.fori_loop(0, steps_here, lambda _, value: step(value), current)

    def forward_work(state):
        forward_packet, adjoint_packet, tangent_out, adjoint_out = state
        advanced = run_steps(step_forward, forward_packet)
        return advanced, adjoint_packet, advanced, adjoint_out

    def adjoint_work(state):
        forward_packet, adjoint_packet, tangent_out, adjoint_out = state
        start_state = (
            seed_panel.astype(jnp.float32) + adjoint_packet.astype(jnp.float32)
        ).astype(jnp.bfloat16)
        advanced = run_steps(step_adjoint, start_state)
        return forward_packet, advanced, tangent_out, advanced

    def compute_round(round_index, state):
        forward_active = position == round_index
        adjoint_active = position == (1 - round_index + seg_count) % seg_count
        branch = jnp.where(forward_active, 1, jnp.where(adjoint_active, 2, 0))
        return lax.switch(branch, [lambda s: s, forward_work, adjoint_work], state)

    def round_body(round_index, state):
        forward_packet, adjoint_packet, tangent_out, adjoint_out = compute_round(
            round_index, state
        )
        forward_packet = shifted_ring(forward_packet, "seg", 1)
        adjoint_packet = shifted_ring(adjoint_packet, "seg", -1)
        return forward_packet, adjoint_packet, tangent_out, adjoint_out

    empty_panel = jnp.zeros_like(start_panel)
    state = (start_panel, empty_panel, empty_panel, empty_panel)
    state = lax.fori_loop(0, seg_count, round_body, state)
    tangent_state, adjoint_state = state[2], state[3]
    chunk_blocks = blocks // dir_size

    both = jnp.stack(
        [
            tangent_state.reshape(dir_size, chunk_blocks, dir_count, block_width),
            adjoint_state.reshape(dir_size, chunk_blocks, dir_count, block_width),
        ],
        axis=1,
    )
    rows_both = lax.all_to_all(both, "dir", split_axis=0, concat_axis=0, tiled=True)
    rows_tangent = rows_both[:, 0]
    rows_adjoint = rows_both[:, 1]
    scale = 1.0 / math.sqrt(blocks * block_width * seg_count)
    partial_gram = jnp.einsum(
        "jbrl,kbql->jrkq", rows_adjoint, rows_tangent, preferred_element_type=jnp.float32
    ).reshape(dir_size * dir_count, dir_size * dir_count) * scale
    by_owner = partial_gram.reshape(dir_size, dir_count, dir_size * dir_count)
    from_chunks = lax.all_to_all(by_owner, "dir", split_axis=0, concat_axis=0, tiled=True)
    projected = lax.psum(jnp.sum(from_chunks, axis=0), "seg")
    return (dir_major(tangent_state)[None], dir_major(adjoint_state)[None], projected)


def solution(mesh):
    in_specs = (
        P("dir", None),
        P("seg", "dir", None),
        P("seg", "dir", None, None),
        P("seg", None, None, None),
        P(),
        P(),
        P(),
    )
    out_specs = (P("seg", "dir", None), P("seg", "dir", None), P("dir", None))
    return jax.shard_map(body, mesh=mesh, in_specs=in_specs, out_specs=out_specs, check_vma=False)
```

```python
import math

import jax
import jax.numpy as jnp
from jax import lax
from jax.sharding import PartitionSpec as P


def shifted_ring(value, axis, steps):
    count = lax.axis_size(axis)
    pairs = [(source, (source + steps) % count) for source in range(count)]
    return lax.ppermute(value, axis, pairs)


def body(panel, seeds, inverses, coupling, weights, pattern, counts):
    blocks = pattern.shape[0]
    couple = pattern.shape[1]
    block_width = coupling.shape[-1]
    dir_count = panel.shape[0]

    def block_major(values):
        return jnp.transpose(values.reshape(dir_count, blocks, block_width), (1, 0, 2))

    def dir_major(values):
        return jnp.transpose(values, (1, 0, 2)).reshape(dir_count, blocks * block_width)

    start_panel = block_major(panel)
    seed_panel = block_major(seeds[0])
    coupling_here = coupling[0]
    seg_count = lax.axis_size("seg")
    position = lax.axis_index("seg")
    steps_here = counts[position]
    dir_size = lax.axis_size("dir")

    inverse_all = lax.all_gather(inverses[0], "dir", axis=0, tiled=True)
    eye = jnp.eye(block_width, dtype=inverse_all.dtype)
    inverse_all_t = jnp.einsum(
        "qk,iek->iqe", eye, inverse_all, preferred_element_type=jnp.float32
    ).astype(inverse_all.dtype)

    pattern_ki = jnp.transpose(pattern).reshape(couple * blocks)
    weights_ki = jnp.transpose(weights).reshape(couple * blocks)
    picker = pattern_ki[:, None] == jnp.arange(blocks, dtype=pattern_ki.dtype)[None, :]
    picker_bf = picker.astype(jnp.bfloat16)

    def step_forward(current):
        picked = jnp.einsum(
            "mj,jrb->mrb", picker_bf, current, preferred_element_type=jnp.float32
        )
        mixed = (picked * weights_ki[:, None, None]).astype(jnp.bfloat16)
        mixed = mixed.reshape(couple, blocks, dir_count, block_width)
        pushed = current.astype(jnp.float32)
        for k in range(couple):
            pushed = pushed + jnp.einsum(
                "nrb,eb->nre", mixed[k], coupling_here[k], preferred_element_type=jnp.float32
            )
        forced = pushed.astype(jnp.bfloat16)
        return jnp.einsum(
            "iqe,irq->ire", inverse_all_t, forced, preferred_element_type=jnp.float32
        ).astype(jnp.bfloat16)

    def step_adjoint(current):
        reached = jnp.einsum(
            "ieq,ire->irq", inverse_all, current, preferred_element_type=jnp.float32
        ).astype(jnp.bfloat16)
        pulled = jnp.stack(
            [
                jnp.einsum(
                    "nre,eb->nrb", reached, coupling_here[k], preferred_element_type=jnp.float32
                ).astype(jnp.bfloat16)
                for k in range(couple)
            ]
        ).reshape(couple * blocks, dir_count, block_width)
        terms = pulled.astype(jnp.float32) * weights_ki[:, None, None]
        terms_hi = terms.astype(jnp.bfloat16)
        terms_lo = (terms - terms_hi.astype(jnp.float32)).astype(jnp.bfloat16)
        spread = jnp.einsum(
            "mj,mrb->jrb", picker_bf, terms_hi, preferred_element_type=jnp.float32
        ) + jnp.einsum("mj,mrb->jrb", picker_bf, terms_lo, preferred_element_type=jnp.float32)
        return (reached.astype(jnp.float32) + spread).astype(jnp.bfloat16)

    def run_steps(step, current):
        return lax.fori_loop(0, steps_here, lambda _, value: step(value), current)

    def forward_work(state):
        forward_packet, adjoint_packet, tangent_out, adjoint_out = state
        advanced = run_steps(step_forward, forward_packet)
        return advanced, adjoint_packet, advanced, adjoint_out

    def adjoint_work(state):
        forward_packet, adjoint_packet, tangent_out, adjoint_out = state
        start_state = (
            seed_panel.astype(jnp.float32) + adjoint_packet.astype(jnp.float32)
        ).astype(jnp.bfloat16)
        advanced = run_steps(step_adjoint, start_state)
        return forward_packet, advanced, tangent_out, advanced

    def compute_round(round_index, state):
        forward_active = position == round_index
        adjoint_active = position == (1 - round_index + seg_count) % seg_count
        branch = jnp.where(forward_active, 1, jnp.where(adjoint_active, 2, 0))
        return lax.switch(branch, [lambda s: s, forward_work, adjoint_work], state)

    def round_body(round_index, state):
        forward_packet, adjoint_packet, tangent_out, adjoint_out = compute_round(
            round_index, state
        )
        forward_packet = shifted_ring(forward_packet, "seg", 1)
        adjoint_packet = shifted_ring(adjoint_packet, "seg", -1)
        return forward_packet, adjoint_packet, tangent_out, adjoint_out

    empty_panel = jnp.zeros_like(start_panel)
    state = (start_panel, empty_panel, empty_panel, empty_panel)
    state = lax.fori_loop(0, seg_count, round_body, state)
    tangent_state, adjoint_state = state[2], state[3]
    chunk_blocks = blocks // dir_size

    both = jnp.stack(
        [
            tangent_state.reshape(dir_size, chunk_blocks, dir_count, block_width),
            adjoint_state.reshape(dir_size, chunk_blocks, dir_count, block_width),
        ],
        axis=1,
    )
    rows_both = lax.all_to_all(both, "dir", split_axis=0, concat_axis=0, tiled=True)
    rows_tangent = rows_both[:, 0]
    rows_adjoint = rows_both[:, 1]
    scale = 1.0 / math.sqrt(blocks * block_width * seg_count)
    partial_gram = jnp.einsum(
        "jbrl,kbql->jrkq", rows_adjoint, rows_tangent, preferred_element_type=jnp.float32
    ).reshape(dir_size * dir_count, dir_size * dir_count) * scale
    by_owner = partial_gram.reshape(dir_size, dir_count, dir_size * dir_count)
    from_chunks = lax.all_to_all(by_owner, "dir", split_axis=0, concat_axis=0, tiled=True)
    projected = lax.psum(jnp.sum(from_chunks, axis=0), "seg")
    return (dir_major(tangent_state)[None], dir_major(adjoint_state)[None], projected)


def solution(mesh):
    in_specs = (
        P("dir", None),
        P("seg", "dir", None),
        P("seg", "dir", None, None),
        P("seg", None, None, None),
        P(),
        P(),
        P(),
    )
    out_specs = (P("seg", "dir", None), P("seg", "dir", None), P("dir", None))
    return jax.shard_map(body, mesh=mesh, in_specs=in_specs, out_specs=out_specs, check_vma=False)
```

```python
import math

import jax
import jax.numpy as jnp
from jax import lax
from jax.sharding import PartitionSpec as P

STEPS_MAX = 2


def shifted_ring(value, axis, steps):
    count = lax.axis_size(axis)
    pairs = [(source, (source + steps) % count) for source in range(count)]
    return lax.ppermute(value, axis, pairs)


def body(panel, seeds, inverses, coupling, weights, pattern, counts):
    blocks = pattern.shape[0]
    couple = pattern.shape[1]
    block_width = coupling.shape[-1]
    dir_count = panel.shape[0]

    def block_major(values):
        return jnp.transpose(values.reshape(dir_count, blocks, block_width), (1, 0, 2))

    def dir_major(values):
        return jnp.transpose(values, (1, 0, 2)).reshape(dir_count, blocks * block_width)

    start_panel = block_major(panel)
    seed_panel = block_major(seeds[0])
    coupling_here = coupling[0]
    seg_count = lax.axis_size("seg")
    position = lax.axis_index("seg")
    steps_here = jnp.clip(counts[position], 0, STEPS_MAX)
    dir_size = lax.axis_size("dir")

    inverse_all = lax.all_gather(inverses[0], "dir", axis=0, tiled=True)
    eye = jnp.eye(block_width, dtype=inverse_all.dtype)
    inverse_all_t = jnp.einsum(
        "qk,iek->iqe", eye, inverse_all, preferred_element_type=jnp.float32
    ).astype(inverse_all.dtype)

    pattern_ki = jnp.transpose(pattern).reshape(couple * blocks)
    weights_ki = jnp.transpose(weights).reshape(couple * blocks)
    picker = pattern_ki[:, None] == jnp.arange(blocks, dtype=pattern_ki.dtype)[None, :]
    picker_bf = picker.astype(jnp.bfloat16)

    def step_forward(current):
        picked = jnp.einsum(
            "mj,jrb->mrb", picker_bf, current, preferred_element_type=jnp.float32
        )
        mixed = (picked * weights_ki[:, None, None]).astype(jnp.bfloat16)
        mixed = mixed.reshape(couple, blocks, dir_count, block_width)
        pushed = current.astype(jnp.float32)
        for k in range(couple):
            pushed = pushed + jnp.einsum(
                "nrb,eb->nre", mixed[k], coupling_here[k], preferred_element_type=jnp.float32
            )
        forced = pushed.astype(jnp.bfloat16)
        return jnp.einsum(
            "iqe,irq->ire", inverse_all_t, forced, preferred_element_type=jnp.float32
        ).astype(jnp.bfloat16)

    def step_adjoint(current):
        reached = jnp.einsum(
            "ieq,ire->irq", inverse_all, current, preferred_element_type=jnp.float32
        ).astype(jnp.bfloat16)
        pulled = jnp.stack(
            [
                jnp.einsum(
                    "nre,eb->nrb", reached, coupling_here[k], preferred_element_type=jnp.float32
                ).astype(jnp.bfloat16)
                for k in range(couple)
            ]
        ).reshape(couple * blocks, dir_count, block_width)
        terms = pulled.astype(jnp.float32) * weights_ki[:, None, None]
        terms_hi = terms.astype(jnp.bfloat16)
        terms_lo = (terms - terms_hi.astype(jnp.float32)).astype(jnp.bfloat16)
        spread = jnp.einsum(
            "mj,mrb->jrb", picker_bf, terms_hi, preferred_element_type=jnp.float32
        ) + jnp.einsum("mj,mrb->jrb", picker_bf, terms_lo, preferred_element_type=jnp.float32)
        return (reached.astype(jnp.float32) + spread).astype(jnp.bfloat16)

    def run_steps(step, current):
        return lax.fori_loop(0, steps_here, lambda _, value: step(value), current)

    def forward_work(state):
        forward_packet, adjoint_packet, tangent_out, adjoint_out = state
        advanced = run_steps(step_forward, forward_packet)
        return advanced, adjoint_packet, advanced, adjoint_out

    def adjoint_work(state):
        forward_packet, adjoint_packet, tangent_out, adjoint_out = state
        start_state = (
            seed_panel.astype(jnp.float32) + adjoint_packet.astype(jnp.float32)
        ).astype(jnp.bfloat16)
        advanced = run_steps(step_adjoint, start_state)
        return forward_packet, advanced, tangent_out, advanced

    def compute_round(round_index, state):
        forward_active = position == round_index
        adjoint_active = position == (1 - round_index + seg_count) % seg_count
        branch = jnp.where(forward_active, 1, jnp.where(adjoint_active, 2, 0))
        return lax.switch(branch, [lambda s: s, forward_work, adjoint_work], state)

    def round_body(round_index, state):
        forward_packet, adjoint_packet, tangent_out, adjoint_out = compute_round(
            round_index, state
        )
        forward_packet = shifted_ring(forward_packet, "seg", 1)
        adjoint_packet = shifted_ring(adjoint_packet, "seg", -1)
        return forward_packet, adjoint_packet, tangent_out, adjoint_out

    empty_panel = jnp.zeros_like(start_panel)
    state = (start_panel, empty_panel, empty_panel, empty_panel)
    state = lax.fori_loop(0, seg_count - 1, round_body, state)
    state = compute_round(seg_count - 1, state)
    tangent_state, adjoint_state = state[2], state[3]
    chunk_blocks = blocks // dir_size

    both = jnp.stack(
        [
            tangent_state.reshape(dir_size, chunk_blocks, dir_count, block_width),
            adjoint_state.reshape(dir_size, chunk_blocks, dir_count, block_width),
        ],
        axis=1,
    )
    rows_both = lax.all_to_all(both, "dir", split_axis=0, concat_axis=0, tiled=True)
    rows_tangent = rows_both[:, 0]
    rows_adjoint = rows_both[:, 1]
    scale = 1.0 / math.sqrt(blocks * block_width * seg_count)
    partial_gram = jnp.einsum(
        "jbrl,kbql->jrkq", rows_adjoint, rows_tangent, preferred_element_type=jnp.float32
    ).reshape(dir_size * dir_count, dir_size * dir_count) * scale
    by_owner = partial_gram.reshape(dir_size, dir_count, dir_size * dir_count)
    from_chunks = lax.all_to_all(by_owner, "dir", split_axis=0, concat_axis=0, tiled=True)
    projected = lax.psum(jnp.sum(from_chunks, axis=0), "seg")
    return (dir_major(tangent_state)[None], dir_major(adjoint_state)[None], projected)


def solution(mesh):
    in_specs = (
        P("dir", None),
        P("seg", "dir", None),
        P("seg", "dir", None, None),
        P("seg", None, None, None),
        P(),
        P(),
        P(),
    )
    out_specs = (P("seg", "dir", None), P("seg", "dir", None), P("dir", None))
    return jax.shard_map(body, mesh=mesh, in_specs=in_specs, out_specs=out_specs, check_vma=False)
```

```python
import math

import jax
import jax.numpy as jnp
from jax import lax
from jax.sharding import PartitionSpec as P

STEPS_MAX = 2


def shifted_ring(value, axis, steps):
    count = lax.axis_size(axis)
    pairs = [(source, (source + steps) % count) for source in range(count)]
    return lax.ppermute(value, axis, pairs)


def body(panel, seeds, inverses, coupling, weights, pattern, counts):
    blocks = pattern.shape[0]
    couple = pattern.shape[1]
    block_width = coupling.shape[-1]
    dir_count = panel.shape[0]

    def block_major(values):
        return jnp.transpose(values.reshape(dir_count, blocks, block_width), (1, 0, 2))

    def dir_major(values):
        return jnp.transpose(values, (1, 0, 2)).reshape(dir_count, blocks * block_width)

    start_panel = block_major(panel)
    seed_panel = block_major(seeds[0])
    coupling_here = coupling[0]
    seg_count = lax.axis_size("seg")
    position = lax.axis_index("seg")
    steps_here = jnp.clip(counts[position], 0, STEPS_MAX)
    dir_size = lax.axis_size("dir")

    inverse_all = lax.all_gather(inverses[0], "dir", axis=0, tiled=True)
    eye = jnp.eye(block_width, dtype=inverse_all.dtype)
    inverse_all_t = jnp.einsum(
        "qk,iek->iqe", eye, inverse_all, preferred_element_type=jnp.float32
    ).astype(inverse_all.dtype)

    pattern_ki = jnp.transpose(pattern).reshape(couple * blocks)
    weights_ki = jnp.transpose(weights).reshape(couple * blocks)
    picker = pattern_ki[:, None] == jnp.arange(blocks, dtype=pattern_ki.dtype)[None, :]
    picker_bf = picker.astype(jnp.bfloat16)

    def step_forward(current):
        picked = jnp.einsum(
            "mj,jrb->mrb", picker_bf, current, preferred_element_type=jnp.float32
        )
        mixed = (picked * weights_ki[:, None, None]).astype(jnp.bfloat16)
        mixed = mixed.reshape(couple, blocks, dir_count, block_width)
        pushed = current.astype(jnp.float32)
        for k in range(couple):
            pushed = pushed + jnp.einsum(
                "nrb,eb->nre", mixed[k], coupling_here[k], preferred_element_type=jnp.float32
            )
        forced = pushed.astype(jnp.bfloat16)
        return jnp.einsum(
            "iqe,irq->ire", inverse_all_t, forced, preferred_element_type=jnp.float32
        ).astype(jnp.bfloat16)

    def step_adjoint(current):
        reached = jnp.einsum(
            "ieq,ire->irq", inverse_all, current, preferred_element_type=jnp.float32
        ).astype(jnp.bfloat16)
        pulled = jnp.stack(
            [
                jnp.einsum(
                    "nre,eb->nrb", reached, coupling_here[k], preferred_element_type=jnp.float32
                ).astype(jnp.bfloat16)
                for k in range(couple)
            ]
        ).reshape(couple * blocks, dir_count, block_width)
        terms = pulled.astype(jnp.float32) * weights_ki[:, None, None]
        terms_hi = terms.astype(jnp.bfloat16)
        terms_lo = (terms - terms_hi.astype(jnp.float32)).astype(jnp.bfloat16)
        spread = jnp.einsum(
            "mj,mrb->jrb", picker_bf, terms_hi, preferred_element_type=jnp.float32
        ) + jnp.einsum("mj,mrb->jrb", picker_bf, terms_lo, preferred_element_type=jnp.float32)
        return (reached.astype(jnp.float32) + spread).astype(jnp.bfloat16)

    def run_steps(step, current):
        return lax.fori_loop(0, steps_here, lambda _, value: step(value), current)

    def forward_work(state):
        forward_packet, adjoint_packet, tangent_out, adjoint_out = state
        advanced = run_steps(step_forward, forward_packet)
        return advanced, adjoint_packet, advanced, adjoint_out

    def adjoint_work(state):
        forward_packet, adjoint_packet, tangent_out, adjoint_out = state
        start_state = (
            seed_panel.astype(jnp.float32) + adjoint_packet.astype(jnp.float32)
        ).astype(jnp.bfloat16)
        advanced = run_steps(step_adjoint, start_state)
        return forward_packet, advanced, tangent_out, advanced

    def compute_round(round_index, state):
        forward_active = position == round_index
        adjoint_active = position == (1 - round_index + seg_count) % seg_count
        branch = jnp.where(forward_active, 1, jnp.where(adjoint_active, 2, 0))
        return lax.switch(branch, [lambda s: s, forward_work, adjoint_work], state)

    def round_body(round_index, state):
        forward_packet, adjoint_packet, tangent_out, adjoint_out = compute_round(
            round_index, state
        )
        forward_packet = shifted_ring(forward_packet, "seg", 1)
        adjoint_packet = shifted_ring(adjoint_packet, "seg", -1)
        return forward_packet, adjoint_packet, tangent_out, adjoint_out

    empty_panel = jnp.zeros_like(start_panel)
    state = (start_panel, empty_panel, empty_panel, empty_panel)
    state = lax.fori_loop(0, seg_count - 1, round_body, state)
    state = compute_round(seg_count - 1, state)
    tangent_state, adjoint_state = state[2], state[3]
    chunk_blocks = blocks // dir_size

    both = jnp.stack(
        [
            tangent_state.reshape(dir_size, chunk_blocks, dir_count, block_width),
            adjoint_state.reshape(dir_size, chunk_blocks, dir_count, block_width),
        ],
        axis=1,
    )
    rows_both = lax.all_to_all(both, "dir", split_axis=0, concat_axis=0, tiled=True)
    rows_tangent = rows_both[:, 0]
    rows_adjoint = rows_both[:, 1]
    scale = 1.0 / math.sqrt(blocks * block_width * seg_count)
    partial_gram = jnp.einsum(
        "jbrl,kbql->jrkq", rows_adjoint, rows_tangent, preferred_element_type=jnp.float32
    ).reshape(dir_size * dir_count, dir_size * dir_count) * scale
    by_owner = partial_gram.reshape(dir_size, dir_count, dir_size * dir_count)
    from_chunks = lax.all_to_all(by_owner, "dir", split_axis=0, concat_axis=0, tiled=True)
    projected = jnp.sum(from_chunks, axis=0)
    distance = 1
    while distance < seg_count:
        pairs = [(source, source ^ distance) for source in range(seg_count)]
        projected = projected + lax.ppermute(projected, "seg", pairs)
        distance *= 2
    return (dir_major(tangent_state)[None], dir_major(adjoint_state)[None], projected)


def solution(mesh):
    in_specs = (
        P("dir", None),
        P("seg", "dir", None),
        P("seg", "dir", None, None),
        P("seg", None, None, None),
        P(),
        P(),
        P(),
    )
    out_specs = (P("seg", "dir", None), P("seg", "dir", None), P("dir", None))
    return jax.shard_map(body, mesh=mesh, in_specs=in_specs, out_specs=out_specs, check_vma=False)
```
